512 devices in a mesh: grp: 4 (over y), seq: 32 (over z, core), mp: 4 (over x).
Axes of the slice: x: 4, y: 4, z: 16, core: 2. Of those that a mesh axis runs over, the one named last changes fastest.
Arguments:
- queries: bfloat16 [4, 4096, 2048], P('grp', 'seq', 'mp'), may hold values from -16 to 16
- d_out: bfloat16 [4, 4096, 2048], P('grp', 'seq', 'mp'), may hold values from -6 to 6
- neighbour_kv: bfloat16 [4, 256, 128, 2, 2048], P('grp', 'seq', None, None, 'mp'), may hold values from -16 to 16
- target: int32 [4, 256], P('grp', 'seq'), may hold values from -1 to 127, as said below
- bias: float32 [16, 191], P('mp'), may hold values from -6 to 6
Outputs:
- attended: bfloat16 [4, 4096, 2048], P('grp', 'seq', 'mp')
- d_query: bfloat16 [4, 4096, 2048], P('grp', 'seq', 'mp')
- d_kv: bfloat16 [4, 256, 128, 2, 2048], P('grp', 'seq', None, None, 'mp')
- d_bias: float32 [16, 191], P('mp')
The draws below stay inside these ranges and needn't reach their ends.
Inputs may be any that keep to these rules, and one draw needn't show every extreme that they name: `target`: in each group every entry 0..127 stands in exactly one slot and -1 marks an empty slot. The slots of one index of seq hold at most 1 entries e with the same e // 4, and some index reaches that; some index of seq holds 8 entries.
All inputs are finite; a program needn't handle non-finite values.
Results may differ from the reference program's by a relative error of at most 0.011.
Values may be sent and summed in bfloat16 or wider, within the bound.
No kernel may reach another device: no remote copies, remote signals or barrier semaphores. Data moves between devices by JAX's collectives and lax.ppermute only.
A program may use at most 128 MiB of HBM per device.

```python
import jax
import jax.numpy as jnp
from jax import lax

HEADS = 16
HD = 128
STRETCH = 64
NB_LEN = 128
CH_DEV = 2
ATTN = 2048
TOKENS_G = 4096
SEQ_LEN = 2048
NB_SLOT = 8
SLOTS_G = 256
REL = 191
N_GRP = 4
N_SEQ = 32


def draw_queries(key, part):
    shape_all = (N_GRP, TOKENS_G, HEADS * HD)
    sample = jnp.clip(jax.random.normal(jax.random.fold_in(key, 11), shape_all, jnp.float32), -6.0, 6.0)
    return sample.astype(jnp.bfloat16)


def draw_neighbour_kv(key, part):
    shape_all = (N_GRP, SLOTS_G, NB_LEN, 2, HEADS * HD)
    sample = jnp.clip(jax.random.normal(jax.random.fold_in(key, 13), shape_all, jnp.float32), -6.0, 6.0)
    return sample.astype(jnp.bfloat16)


def group_targets(key):
    per_owner = 2 * CH_DEV
    group_size = min(N_SEQ, per_owner)
    full_count = NB_SLOT
    entry_total = per_owner * N_SEQ
    others = N_SEQ - group_size
    full_part = jnp.full((group_size,), full_count, jnp.int32)
    if others > 0:
        remain = entry_total - group_size * full_count
        base_count = remain // others
        extra = remain % others
        counts_rest = base_count + (jnp.arange(others) < extra).astype(jnp.int32)
        pair_count = others // 2
        if pair_count > 0:
            reach = min(base_count, full_count - base_count - 1)
            moves = jax.random.randint(jax.random.fold_in(key, 1), (pair_count,), 0, reach + 1).astype(jnp.int32)
            change = jnp.zeros((others,), jnp.int32)
            change = change.at[0:2 * pair_count:2].add(moves).at[1:2 * pair_count:2].add(-moves)
            counts_rest = counts_rest + change
        counts_pos = jnp.concatenate([full_part, counts_rest])
    else:
        counts_pos = full_part
    shard_perm = jax.random.permutation(jax.random.fold_in(key, 2), N_SEQ)
    counts = jnp.zeros((N_SEQ,), jnp.int32).at[shard_perm].set(counts_pos)
    slot_ids = jnp.arange(full_count)
    above = (counts[None, :] > slot_ids[:, None]).astype(jnp.int32)
    per_round = jnp.sum(above, axis=1)
    round_start = jnp.cumsum(per_round) - per_round
    within = jnp.cumsum(above, axis=1) - above
    entries = jnp.where(above > 0, round_start[:, None] + within, -1).T
    shard_keys = jax.random.split(jax.random.fold_in(key, 3), N_SEQ)
    slot_perm = jax.vmap(lambda sub: jax.random.permutation(sub, full_count))(shard_keys)
    placed = jnp.zeros((N_SEQ, full_count), jnp.int32).at[jnp.arange(N_SEQ)[:, None], slot_perm].set(entries)
    return placed.reshape(N_SEQ * full_count)


def draw_target(key, part):
    group_keys = jax.random.split(jax.random.fold_in(key, 77), N_GRP)
    return jax.vmap(group_targets)(group_keys).astype(jnp.int32)


def block_levels(rng, extent, cuts, low, top_value):
    def one(position, parts):
        steps = jax.random.uniform(jax.random.fold_in(jax.random.fold_in(rng, 6), position), (parts,), jnp.float32, low / len(cuts), top_value / len(cuts))
        return jnp.repeat(jnp.exp(steps), extent[position] // parts).reshape((-1,) + (1,) * (len(extent) - position - 1))

    level = one(*cuts[0])
    for cut in cuts[1:]:
        level = level * one(*cut)
    return level


def noise(rng, shape, deviation, most, cuts=(), kind=jnp.bfloat16):
    result = jax.random.normal(rng, shape, jnp.float32) * deviation
    if len(cuts) > 0:
        result = block_levels(rng, shape, cuts, -0.22, 0.18) * result
    return jnp.clip(result, min=-most, max=most).astype(kind)


def setup_inputs(seed: int = 0) -> dict:
    arg_keys = jax.random.split(jax.random.key(seed), 6)
    queries = draw_queries(jax.random.fold_in(arg_keys[5], 71), 0)
    d_out = noise(arg_keys[1], (N_GRP, TOKENS_G, ATTN), 1.0, 6.0, ((0, 4), (1, 32), (2, 4)))
    neighbour_kv = draw_neighbour_kv(jax.random.fold_in(arg_keys[5], 71), 0)
    target = draw_target(jax.random.fold_in(arg_keys[5], 71), 0)
    bias = noise(arg_keys[4], (HEADS, REL), 1.0, 6.0, ((0, 4),), jnp.float32)
    return {"queries": queries, "d_out": d_out, "neighbour_kv": neighbour_kv, "target": target, "bias": bias}


def bias_grid(lookup, row_count, col_count):
    head_num = lookup.shape[0]
    span = row_count + col_count
    padded = jnp.pad(lookup, ((0, 0), (0, 1)))
    flattened = jnp.tile(padded, (1, row_count))
    flattened = jnp.pad(flattened, ((0, 0), (0, row_count)))
    shaped = flattened.reshape(head_num, row_count, span + 1)[:, :, :col_count]
    return shaped[:, :, ::-1]

def bias_fold(grads):
    head_num, row_count, col_count = grads.shape
    turned = grads[:, :, ::-1]
    padded = jnp.pad(turned, ((0, 0), (0, 0), (0, row_count)))
    flattened = padded.reshape(head_num, row_count * (row_count + col_count))
    flattened = flattened[:, :row_count * (row_count + col_count - 1)]
    return lax.optimization_barrier(jnp.sum(flattened.reshape(head_num, row_count, row_count + col_count - 1), axis=1))

def to_wide(values_in):
    return lax.optimization_barrier(values_in.astype(jnp.bfloat16)).astype(jnp.float32)

def window_math(q_rows, g_rows, key_rows, value_rows, grid_rows, scale_factor, live_row):
    q_wide = q_rows.astype(jnp.float32)
    g_wide = g_rows.astype(jnp.float32)
    k_wide = key_rows.astype(jnp.float32)
    v_wide = value_rows.astype(jnp.float32)
    scores = jnp.einsum('ihd,njhd->nihj', q_wide, k_wide) * scale_factor + grid_rows[None]
    peak_val = lax.optimization_barrier(jnp.max(scores, axis=-1))
    weights = jnp.exp(scores - peak_val[..., None])
    row_total = lax.optimization_barrier(jnp.sum(weights, axis=-1))
    partial_value = jnp.einsum('nihj,njhd->nihd', to_wide(weights), v_wide)
    top_peak = lax.optimization_barrier(jnp.max(peak_val, axis=0))
    factor = jnp.exp(peak_val - top_peak[None])
    denominator = lax.optimization_barrier(jnp.sum(factor * row_total, axis=0))
    combined = lax.optimization_barrier(jnp.sum(factor[..., None] * partial_value, axis=0)) / denominator[..., None]
    combined = combined * live_row[:, None, None]
    log_total = top_peak + jnp.log(denominator)
    inner_dot = lax.optimization_barrier(jnp.sum(g_wide * combined, axis=-1))
    prob_full = jnp.exp(scores - log_total[None, ..., None])
    grad_values = jnp.einsum('nihj,ihd->njhd', to_wide(prob_full), g_wide)
    grad_prob = jnp.einsum('ihd,njhd->nihj', g_wide, v_wide)
    grad_scores = prob_full * (grad_prob - inner_dot[None, ..., None])
    scores_low = to_wide(grad_scores)
    grad_rows = jnp.einsum('nihj,njhd->ihd', scores_low, k_wide) * scale_factor
    grad_keys = jnp.einsum('nihj,ihd->njhd', scores_low, q_wide) * scale_factor
    bias_part = bias_fold(lax.optimization_barrier(jnp.sum(grad_scores, axis=0)).transpose(1, 0, 2))
    return (combined, grad_rows, grad_keys, grad_values, bias_part)

def reference(queries, d_out, neighbour_kv, target, bias):
    groups, tokens, full_width = queries.shape
    head_num = bias.shape[0]
    head_depth = full_width // head_num
    stretches = tokens // STRETCH
    seq_stretches = SEQ_LEN // STRETCH
    scale_factor = head_depth ** (-0.5)
    grid_rows = bias_grid(bias, STRETCH, NB_LEN).transpose(1, 0, 2)
    row_ids = jnp.arange(STRETCH)
    stretch_ids = jnp.arange(stretches)
    live_rows = ((row_ids[None, :] == 0) | ((stretch_ids[:, None] + 1) % seq_stretches != 0)).astype(jnp.float32)

    def one_group(group_idx):
        q_group = queries[group_idx]
        g_group = d_out[group_idx]
        kv_group = neighbour_kv[group_idx]
        t_group = target[group_idx]
        padding = jnp.zeros((STRETCH, full_width), queries.dtype)
        q_win = jnp.concatenate([q_group, padding])[STRETCH - 1:STRETCH - 1 + tokens]
        q_win = q_win.reshape(stretches, STRETCH, head_num, head_depth)
        g_win = jnp.concatenate([g_group, padding])[STRETCH - 1:STRETCH - 1 + tokens]
        g_win = g_win.reshape(stretches, STRETCH, head_num, head_depth) * live_rows[:, :, None, None].astype(d_out.dtype)
        entry_ids = jnp.arange(2 * stretches, dtype=jnp.int32)
        slot_of = jnp.argmax(t_group[None, :] == entry_ids[:, None], axis=1).astype(jnp.int32)
        blocks = kv_group[slot_of].reshape(stretches, 2, NB_LEN, 2, head_num, head_depth)

        def one_stretch(item):
            q_rows, g_rows, block, live_row = item
            combined, grad_rows, grad_keys, grad_values, bias_part = window_math(q_rows, g_rows, block[:, :, 0], block[:, :, 1], grid_rows, scale_factor, live_row)
            stacked = jnp.stack([grad_keys, grad_values], axis=2).astype(jnp.bfloat16)
            return (combined.astype(jnp.bfloat16), grad_rows.astype(jnp.bfloat16), stacked, bias_part)
        outs_win, grads_win, kv_grads, bias_parts = lax.map(one_stretch, (q_win, g_win, blocks, live_rows))
        lead = jnp.zeros((STRETCH - 1, full_width), jnp.bfloat16)
        attended = jnp.concatenate([lead, outs_win.reshape(tokens, full_width)[:tokens - STRETCH + 1]])
        d_query = jnp.concatenate([lead, grads_win.reshape(tokens, full_width)[:tokens - STRETCH + 1]])
        kv_entries = kv_grads.reshape(2 * stretches, NB_LEN, 2, full_width)
        slot_mask = (t_group >= 0).astype(jnp.bfloat16)
        d_kv = kv_entries[jnp.clip(t_group, 0, 2 * stretches - 1)] * slot_mask[:, None, None, None]
        return (attended, d_query, d_kv, lax.optimization_barrier(jnp.sum(bias_parts, axis=0)))
    attended, d_query, d_kv, bias_groups = lax.map(one_group, jnp.arange(groups))
    raw_sum = lax.optimization_barrier(jnp.sum(bias_groups, axis=0))
    norm_val = jnp.sqrt(jnp.sum(raw_sum * raw_sum) + 1e-12)
    d_bias = raw_sum * jnp.minimum(1.0, 1.0 / norm_val)
    return (attended, d_query, d_kv, d_bias)
```

```python
import jax
import jax.numpy as jnp
from jax import lax
from jax.sharding import PartitionSpec as P

STRETCH = 64
NB_LEN = 128
SEQ_LEN = 2048


def passed_along(block, axis, distance):
    devices = range(lax.axis_size(axis))
    route = [(i - distance, i) for i in devices if i - distance in devices]
    return lax.ppermute(block, axis, route)


def bias_grid(lookup, row_count, col_count):
    head_num = lookup.shape[0]
    span = row_count + col_count
    padded = jnp.pad(lookup, ((0, 0), (0, 1)))
    flattened = jnp.tile(padded, (1, row_count))
    flattened = jnp.pad(flattened, ((0, 0), (0, row_count)))
    shaped = flattened.reshape(head_num, row_count, span + 1)[:, :, :col_count]
    return shaped[:, :, ::-1]


def bias_fold(grads):
    head_num, row_count, col_count = grads.shape
    turned = grads[:, :, ::-1]
    padded = jnp.pad(turned, ((0, 0), (0, 0), (0, row_count)))
    flattened = padded.reshape(head_num, row_count * (row_count + col_count))
    flattened = flattened[:, : row_count * (row_count + col_count - 1)]
    return jnp.sum(flattened.reshape(head_num, row_count, row_count + col_count - 1), axis=1)


def take_rows(table, index, valid):
    rows = jnp.take(table, index, axis=0)
    shape = (valid.shape[0],) + (1,) * (rows.ndim - 1)
    return jnp.where(valid.reshape(shape), rows, jnp.zeros((), rows.dtype))


def exchange(block):
    return lax.all_to_all(block, "seq", split_axis=0, concat_axis=0, tiled=True)


def local(queries, d_out, neighbour_kv, target, bias):
    tok_rows = queries.shape[1]
    width_dev = queries.shape[2]
    head_count = bias.shape[0]
    head_depth = width_dev // head_count
    stretch_count = tok_rows // STRETCH
    per_owner = 2 * stretch_count
    shard_count = lax.axis_size("seq")
    my_index = lax.axis_index("seq")
    group_rows = tok_rows * shard_count
    seq_stretches = min(SEQ_LEN, group_rows) // STRETCH
    scale_factor = head_depth ** (-0.5)
    bias_rows = bias_grid(bias, STRETCH, NB_LEN).transpose(1, 0, 2)
    row_ids = jnp.arange(STRETCH)

    q_all = lax.all_gather(queries[0], "seq", axis=0, tiled=True)
    g_all = lax.all_gather(d_out[0], "seq", axis=0, tiled=True)

    my_targets = target[0]
    slot_count = my_targets.shape[0]
    is_used = my_targets >= 0
    entry = jnp.where(is_used, my_targets, 0)
    stretch_of = entry // 2
    win_rows = stretch_of[:, None] * STRETCH + (STRETCH - 1) + row_ids[None, :]
    in_group = win_rows < group_rows
    win_rows = jnp.minimum(win_rows.reshape(-1), group_rows - 1)
    q_win = jnp.take(q_all, win_rows, axis=0).reshape(slot_count, STRETCH, width_dev)
    g_win = jnp.take(g_all, win_rows, axis=0).reshape(slot_count, STRETCH, width_dev)
    live_slot = (row_ids[None, :] == 0) | ((stretch_of[:, None] + 1) % seq_stretches != 0)
    q_keep = is_used[:, None] & in_group
    q_slots = jnp.where(q_keep[:, :, None], q_win, jnp.zeros((), q_win.dtype))
    g_slots = jnp.where((q_keep & live_slot)[:, :, None], g_win, jnp.zeros((), g_win.dtype))
    q_slots = q_slots.reshape(slot_count, STRETCH, head_count, head_depth)
    g_slots = g_slots.reshape(slot_count, STRETCH, head_count, head_depth)

    stored = neighbour_kv[0]
    key_rows = stored[:, :, 0].reshape(slot_count, NB_LEN, head_count, head_depth)
    value_rows = stored[:, :, 1].reshape(slot_count, NB_LEN, head_count, head_depth)
    scores = jnp.einsum("sihd,sjhd->sihj", q_slots, key_rows, preferred_element_type=jnp.float32)
    scores = scores * scale_factor + bias_rows[None]
    peak_val = jnp.max(scores, axis=-1)
    weights = jnp.exp(scores - peak_val[..., None])
    row_total = jnp.sum(weights, axis=-1)
    partial_value = jnp.einsum(
        "sihj,sjhd->sihd",
        weights.astype(jnp.bfloat16),
        value_rows,
        preferred_element_type=jnp.float32,
    )

    owner_of = jnp.where(is_used, my_targets // per_owner, -1)
    owner_match = owner_of[None, :] == jnp.arange(shard_count)[:, None]
    send_slot = jnp.argmax(owner_match, axis=1)
    send_has = jnp.any(owner_match, axis=1)
    part_send = take_rows(
        partial_value.astype(jnp.bfloat16).reshape(slot_count, STRETCH, width_dev), send_slot, send_has
    )
    slot_stats = jnp.concatenate(
        [
            jnp.stack([peak_val, row_total], axis=1).reshape(slot_count, -1),
            (entry + 1).astype(jnp.float32)[:, None],
        ],
        axis=1,
    )
    stat_send = take_rows(slot_stats, send_slot, send_has)
    part_recv = exchange(part_send)
    stat_recv = exchange(stat_send)

    own_entries = my_index * per_owner + jnp.arange(per_owner)
    sent_ids = stat_recv[:, -1].astype(jnp.int32) - 1
    where_held = sent_ids[None, :] == own_entries[:, None]
    held_by = jnp.argmax(where_held, axis=1)
    parts_own = jnp.take(part_recv, held_by, axis=0).astype(jnp.float32)
    parts_own = parts_own.reshape(stretch_count, 2, STRETCH, head_count, head_depth)
    stats_own = jnp.take(stat_recv[:, :-1], held_by, axis=0)
    stats_own = stats_own.reshape(stretch_count, 2, 2, STRETCH, head_count)
    peaks_own = stats_own[:, :, 0]
    totals_own = stats_own[:, :, 1]

    stretch_ids = my_index * stretch_count + jnp.arange(stretch_count)
    is_live = (row_ids[None, :] == 0) | ((stretch_ids[:, None] + 1) % seq_stretches != 0)
    live_rows = is_live.astype(jnp.float32)
    top_peak = jnp.max(peaks_own, axis=1)
    factor = jnp.exp(peaks_own - top_peak[:, None])
    denominator = jnp.sum(factor * totals_own, axis=1)
    combined = jnp.sum(factor[..., None] * parts_own, axis=1) / denominator[..., None]
    combined = combined * live_rows[:, :, None, None]
    att_win = combined.astype(jnp.bfloat16).reshape(tok_rows, width_dev)
    att_before = passed_along(att_win[tok_rows - STRETCH :], "seq", 1)

    g_dot = jnp.einsum(
        "sihd,sihd->sih", g_slots.astype(jnp.float32), partial_value, precision=lax.Precision.HIGHEST
    )
    mine = jnp.stack([peak_val, row_total, g_dot], axis=1)
    shared = jnp.concatenate(
        [mine.reshape(slot_count, -1), jnp.where(is_used, entry + 1, 0).astype(jnp.float32)[:, None]],
        axis=1,
    )
    shared_all = lax.all_gather(shared, "seq", tiled=True)
    partner = entry + 1 - 2 * (entry % 2)
    partner_at = jnp.argmax(shared_all[None, :, -1] == (partner + 1).astype(jnp.float32)[:, None], axis=1)
    theirs = jnp.take(shared_all[:, :-1], partner_at, axis=0).reshape(mine.shape)
    both_peak = jnp.maximum(mine[:, 0], theirs[:, 0])
    mine_f = jnp.exp(mine[:, 0] - both_peak)
    theirs_f = jnp.exp(theirs[:, 0] - both_peak)
    both_total = mine_f * mine[:, 1] + theirs_f * theirs[:, 1]
    lse_slots = both_peak + jnp.log(both_total)
    dd_slots = (mine_f * mine[:, 2] + theirs_f * theirs[:, 2]) / both_total
    dd_slots = jnp.where(is_used[:, None, None], dd_slots, 0.0)
    prob_full = jnp.exp(scores - lse_slots[..., None])
    prob_low = prob_full.astype(jnp.bfloat16)
    grad_prob = jnp.einsum(
        "sihd,sjhd->sihj", g_slots, value_rows, preferred_element_type=jnp.float32
    )
    grad_scores = prob_full * (grad_prob - dd_slots[..., None])
    scores_low = grad_scores.astype(jnp.bfloat16)
    grad_rows = (
        jnp.einsum("sihj,sjhd->sihd", scores_low, key_rows, preferred_element_type=jnp.float32)
        * scale_factor
    )
    mix_probs = jnp.stack([scores_low, prob_low], axis=1)
    mix_rows = jnp.stack([q_slots, g_slots], axis=1)
    grad_kv = jnp.einsum("sxihj,sxihd->sjxhd", mix_probs, mix_rows, preferred_element_type=jnp.float32)
    kv_scale = jnp.array([scale_factor, 1.0], jnp.float32)[None, None, :, None, None]
    d_kv = (grad_kv * kv_scale).astype(jnp.bfloat16).reshape(slot_count, NB_LEN, 2, width_dev)
    bias_part = bias_fold(jnp.sum(grad_scores, axis=0).transpose(1, 0, 2))

    dq_rows = jnp.zeros((shard_count, stretch_count, STRETCH, width_dev), jnp.bfloat16)
    dq_owner = jnp.where(is_used, owner_of, shard_count)
    dq_rows = dq_rows.at[dq_owner, stretch_of % stretch_count].set(
        grad_rows.astype(jnp.bfloat16).reshape(slot_count, STRETCH, width_dev), mode="drop"
    )
    grad_win = lax.psum_scatter(dq_rows, "seq", scatter_dimension=0, tiled=True)
    grad_win = grad_win.reshape(tok_rows, width_dev)
    grad_before = passed_along(grad_win[tok_rows - STRETCH :], "seq", 1)
    attended = jnp.concatenate([att_before[1:], att_win[: tok_rows - STRETCH + 1]])
    d_query = jnp.concatenate([grad_before[1:], grad_win[: tok_rows - STRETCH + 1]])

    raw_sum = lax.psum(lax.psum(bias_part, "seq"), "grp")
    squares = lax.psum(jnp.sum(raw_sum * raw_sum), "mp")
    d_bias = raw_sum * jnp.minimum(1.0, 1.0 / jnp.sqrt(squares + 1e-12))
    return (attended[None], d_query[None], d_kv[None], d_bias)


def solution(mesh):
    in_specs = (
        P("grp", "seq", "mp"),
        P("grp", "seq", "mp"),
        P("grp", "seq", None, None, "mp"),
        P("grp", "seq"),
        P("mp", None),
    )
    out_specs = (
        P("grp", "seq", "mp"),
        P("grp", "seq", "mp"),
        P("grp", "seq", None, None, "mp"),
        P("mp", None),
    )
    return jax.shard_map(local, mesh=mesh, in_specs=in_specs, out_specs=out_specs, check_vma=False)
```

```python
import jax
import jax.numpy as jnp
from jax import lax
from jax.sharding import PartitionSpec as P

STRETCH = 64
NB_LEN = 128
SEQ_LEN = 2048


def passed_along(block, axis, distance):
    devices = range(lax.axis_size(axis))
    route = [(i - distance, i) for i in devices if i - distance in devices]
    return lax.ppermute(block, axis, route)


def bias_grid(lookup, row_count, col_count):
    head_num = lookup.shape[0]
    span = row_count + col_count
    padded = jnp.pad(lookup, ((0, 0), (0, 1)))
    flattened = jnp.tile(padded, (1, row_count))
    flattened = jnp.pad(flattened, ((0, 0), (0, row_count)))
    shaped = flattened.reshape(head_num, row_count, span + 1)[:, :, :col_count]
    return shaped[:, :, ::-1]


def bias_fold(grads):
    head_num, row_count, col_count = grads.shape
    turned = grads[:, :, ::-1]
    padded = jnp.pad(turned, ((0, 0), (0, 0), (0, row_count)))
    flattened = padded.reshape(head_num, row_count * (row_count + col_count))
    flattened = flattened[:, : row_count * (row_count + col_count - 1)]
    return jnp.sum(flattened.reshape(head_num, row_count, row_count + col_count - 1), axis=1)


def take_rows(table, index, valid):
    rows = jnp.take(table, index, axis=0)
    shape = (valid.shape[0],) + (1,) * (rows.ndim - 1)
    return jnp.where(valid.reshape(shape), rows, jnp.zeros((), rows.dtype))


def exchange(block):
    return lax.all_to_all(block, "seq", split_axis=0, concat_axis=0, tiled=True)


def local(queries, d_out, neighbour_kv, target, bias):
    tok_rows = queries.shape[1]
    width_dev = queries.shape[2]
    head_count = bias.shape[0]
    head_depth = width_dev // head_count
    stretch_count = tok_rows // STRETCH
    per_owner = 2 * stretch_count
    shard_count = lax.axis_size("seq")
    my_index = lax.axis_index("seq")
    group_rows = tok_rows * shard_count
    seq_stretches = min(SEQ_LEN, group_rows) // STRETCH
    scale_factor = head_depth ** (-0.5)
    bias_rows = bias_grid(bias, STRETCH, NB_LEN).transpose(1, 0, 2)
    row_ids = jnp.arange(STRETCH)

    pair = jnp.stack([queries[0], d_out[0]], axis=1)
    pair_all = lax.all_gather(pair, "seq", axis=0, tiled=True)

    my_targets = target[0]
    slot_count = my_targets.shape[0]
    is_used = my_targets >= 0
    entry = jnp.where(is_used, my_targets, 0)
    stretch_of = entry // 2
    win_rows = stretch_of[:, None] * STRETCH + (STRETCH - 1) + row_ids[None, :]
    in_group = win_rows < group_rows
    win_rows = jnp.minimum(win_rows.reshape(-1), group_rows - 1)
    win = jnp.take(pair_all, win_rows, axis=0).reshape(slot_count, STRETCH, 2, width_dev)
    q_win = win[:, :, 0]
    g_win = win[:, :, 1]
    live_slot = (row_ids[None, :] == 0) | ((stretch_of[:, None] + 1) % seq_stretches != 0)
    q_keep = is_used[:, None] & in_group
    q_slots = jnp.where(q_keep[:, :, None], q_win, jnp.zeros((), q_win.dtype))
    g_slots = jnp.where((q_keep & live_slot)[:, :, None], g_win, jnp.zeros((), g_win.dtype))
    q_slots = q_slots.reshape(slot_count, STRETCH, head_count, head_depth)
    g_slots = g_slots.reshape(slot_count, STRETCH, head_count, head_depth)

    stored = neighbour_kv[0]
    key_rows = stored[:, :, 0].reshape(slot_count, NB_LEN, head_count, head_depth)
    value_rows = stored[:, :, 1].reshape(slot_count, NB_LEN, head_count, head_depth)
    scores = jnp.einsum("sihd,sjhd->sihj", q_slots, key_rows, preferred_element_type=jnp.float32)
    scores = scores * scale_factor + bias_rows[None]
    peak_val = jnp.max(scores, axis=-1)
    weights = jnp.exp(scores - peak_val[..., None])
    row_total = jnp.sum(weights, axis=-1)
    partial_value = jnp.einsum(
        "sihj,sjhd->sihd",
        weights.astype(jnp.bfloat16),
        value_rows,
        preferred_element_type=jnp.float32,
    )

    owner_of = jnp.where(is_used, my_targets // per_owner, -1)
    owner_match = owner_of[None, :] == jnp.arange(shard_count)[:, None]
    send_slot = jnp.argmax(owner_match, axis=1)
    send_has = jnp.any(owner_match, axis=1)
    part_send = take_rows(
        partial_value.astype(jnp.bfloat16).reshape(slot_count, STRETCH, width_dev), send_slot, send_has
    )
    g_dot = jnp.einsum(
        "sihd,sihd->sih", g_slots.astype(jnp.float32), partial_value, precision=lax.Precision.HIGHEST
    )
    mine = jnp.stack([peak_val, row_total, g_dot], axis=1)
    shared = jnp.concatenate(
        [mine.reshape(slot_count, -1), jnp.where(is_used, entry + 1, 0).astype(jnp.float32)[:, None]],
        axis=1,
    )
    shared_all = lax.all_gather(shared, "seq", tiled=True)
    partner = entry + 1 - 2 * (entry % 2)
    partner_at = jnp.argmax(shared_all[None, :, -1] == (partner + 1).astype(jnp.float32)[:, None], axis=1)
    theirs = jnp.take(shared_all[:, :-1], partner_at, axis=0).reshape(mine.shape)
    both_peak = jnp.maximum(mine[:, 0], theirs[:, 0])
    mine_f = jnp.exp(mine[:, 0] - both_peak)
    theirs_f = jnp.exp(theirs[:, 0] - both_peak)
    both_total = mine_f * mine[:, 1] + theirs_f * theirs[:, 1]
    lse_slots = both_peak + jnp.log(both_total)
    dd_slots = (mine_f * mine[:, 2] + theirs_f * theirs[:, 2]) / both_total
    dd_slots = jnp.where(is_used[:, None, None], dd_slots, 0.0)

    part_recv = exchange(part_send)

    own_entries = my_index * per_owner + jnp.arange(per_owner)
    own_at = jnp.argmax(shared_all[None, :, -1] == (own_entries + 1).astype(jnp.float32)[:, None], axis=1)
    held_by = own_at // slot_count
    parts_own = jnp.take(part_recv, held_by, axis=0).astype(jnp.float32)
    parts_own = parts_own.reshape(stretch_count, 2, STRETCH, head_count, head_depth)
    stats_own = jnp.take(shared_all[:, :-1], own_at, axis=0).reshape(stretch_count, 2, 3, STRETCH, head_count)
    peaks_own = stats_own[:, :, 0]
    totals_own = stats_own[:, :, 1]

    stretch_ids = my_index * stretch_count + jnp.arange(stretch_count)
    is_live = (row_ids[None, :] == 0) | ((stretch_ids[:, None] + 1) % seq_stretches != 0)
    live_rows = is_live.astype(jnp.float32)
    top_peak = jnp.max(peaks_own, axis=1)
    factor = jnp.exp(peaks_own - top_peak[:, None])
    denominator = jnp.sum(factor * totals_own, axis=1)
    combined = jnp.sum(factor[..., None] * parts_own, axis=1) / denominator[..., None]
    combined = combined * live_rows[:, :, None, None]
    att_win = combined.astype(jnp.bfloat16).reshape(tok_rows, width_dev)
    att_before = passed_along(att_win[tok_rows - STRETCH :], "seq", 1)

    prob_full = jnp.exp(scores - lse_slots[..., None])
    prob_low = prob_full.astype(jnp.bfloat16)
    grad_prob = jnp.einsum(
        "sihd,sjhd->sihj", g_slots, value_rows, preferred_element_type=jnp.float32
    )
    grad_scores = prob_full * (grad_prob - dd_slots[..., None])
    scores_low = grad_scores.astype(jnp.bfloat16)
    grad_rows = (
        jnp.einsum("sihj,sjhd->sihd", scores_low, key_rows, preferred_element_type=jnp.float32)
        * scale_factor
    )
    mix_probs = jnp.stack([scores_low, prob_low], axis=1)
    mix_rows = jnp.stack([q_slots, g_slots], axis=1)
    grad_kv = jnp.einsum("sxihj,sxihd->sjxhd", mix_probs, mix_rows, preferred_element_type=jnp.float32)
    kv_scale = jnp.array([scale_factor, 1.0], jnp.float32)[None, None, :, None, None]
    d_kv = (grad_kv * kv_scale).astype(jnp.bfloat16).reshape(slot_count, NB_LEN, 2, width_dev)
    bias_part = bias_fold(jnp.sum(grad_scores, axis=0).transpose(1, 0, 2))

    dq_rows = jnp.zeros((shard_count, stretch_count, STRETCH, width_dev), jnp.bfloat16)
    dq_owner = jnp.where(is_used, owner_of, shard_count)
    dq_rows = dq_rows.at[dq_owner, stretch_of % stretch_count].set(
        grad_rows.astype(jnp.bfloat16).reshape(slot_count, STRETCH, width_dev), mode="drop"
    )
    grad_win = lax.psum_scatter(dq_rows, "seq", scatter_dimension=0, tiled=True)
    grad_win = grad_win.reshape(tok_rows, width_dev)
    grad_before = passed_along(grad_win[tok_rows - STRETCH :], "seq", 1)
    attended = jnp.concatenate([att_before[1:], att_win[: tok_rows - STRETCH + 1]])
    d_query = jnp.concatenate([grad_before[1:], grad_win[: tok_rows - STRETCH + 1]])

    raw_sum = lax.psum(lax.psum(bias_part, "seq"), "grp")
    squares = lax.psum(jnp.sum(raw_sum * raw_sum), "mp")
    d_bias = raw_sum * jnp.minimum(1.0, 1.0 / jnp.sqrt(squares + 1e-12))
    return (attended[None], d_query[None], d_kv[None], d_bias)


def solution(mesh):
    in_specs = (
        P("grp", "seq", "mp"),
        P("grp", "seq", "mp"),
        P("grp", "seq", None, None, "mp"),
        P("grp", "seq"),
        P("mp", None),
    )
    out_specs = (
        P("grp", "seq", "mp"),
        P("grp", "seq", "mp"),
        P("grp", "seq", None, None, "mp"),
        P("mp", None),
    )
    return jax.shard_map(local, mesh=mesh, in_specs=in_specs, out_specs=out_specs, check_vma=False)
```

```python
import jax
import jax.numpy as jnp
from jax import lax
from jax.sharding import PartitionSpec as P

STRETCH = 64
NB_LEN = 128
SEQ_LEN = 2048


def passed_along(block, axis, distance):
    devices = range(lax.axis_size(axis))
    route = [(i - distance, i) for i in devices if i - distance in devices]
    return lax.ppermute(block, axis, route)


def bias_grid(lookup, row_count, col_count):
    head_num = lookup.shape[0]
    span = row_count + col_count
    padded = jnp.pad(lookup, ((0, 0), (0, 1)))
    flattened = jnp.tile(padded, (1, row_count))
    flattened = jnp.pad(flattened, ((0, 0), (0, row_count)))
    shaped = flattened.reshape(head_num, row_count, span + 1)[:, :, :col_count]
    return shaped[:, :, ::-1]


def bias_fold(grads):
    head_num, row_count, col_count = grads.shape
    turned = grads[:, :, ::-1]
    padded = jnp.pad(turned, ((0, 0), (0, 0), (0, row_count)))
    flattened = padded.reshape(head_num, row_count * (row_count + col_count))
    flattened = flattened[:, : row_count * (row_count + col_count - 1)]
    return jnp.sum(flattened.reshape(head_num, row_count, row_count + col_count - 1), axis=1)


def take_rows(table, index, valid):
    rows = jnp.take(table, index, axis=0)
    shape = (valid.shape[0],) + (1,) * (rows.ndim - 1)
    return jnp.where(valid.reshape(shape), rows, jnp.zeros((), rows.dtype))


def exchange(block):
    return lax.all_to_all(block, "seq", split_axis=0, concat_axis=0, tiled=True)


def local(queries, d_out, neighbour_kv, target, bias):
    tok_rows = queries.shape[1]
    width_dev = queries.shape[2]
    head_count = bias.shape[0]
    head_depth = width_dev // head_count
    stretch_count = tok_rows // STRETCH
    per_owner = 2 * stretch_count
    shard_count = lax.axis_size("seq")
    my_index = lax.axis_index("seq")
    group_rows = tok_rows * shard_count
    seq_stretches = min(SEQ_LEN, group_rows) // STRETCH
    scale_factor = head_depth ** (-0.5)
    bias_rows = bias_grid(bias, STRETCH, NB_LEN).transpose(1, 0, 2)
    row_ids = jnp.arange(STRETCH)

    pair = jnp.stack([queries[0], d_out[0]], axis=1)
    pair_all = lax.all_gather(pair, "seq", axis=0, tiled=True)

    my_targets = target[0]
    slot_count = my_targets.shape[0]
    is_used = my_targets >= 0
    entry = jnp.where(is_used, my_targets, 0)
    stretch_of = entry // 2
    win_rows = stretch_of[:, None] * STRETCH + (STRETCH - 1) + row_ids[None, :]
    in_group = win_rows < group_rows
    win_rows = jnp.minimum(win_rows.reshape(-1), group_rows - 1)
    win = jnp.take(pair_all, win_rows, axis=0).reshape(slot_count, STRETCH, 2, width_dev)
    q_win = win[:, :, 0]
    g_win = win[:, :, 1]
    live_slot = (row_ids[None, :] == 0) | ((stretch_of[:, None] + 1) % seq_stretches != 0)
    q_keep = is_used[:, None] & in_group
    q_slots = jnp.where(q_keep[:, :, None], q_win, jnp.zeros((), q_win.dtype))
    g_slots = jnp.where((q_keep & live_slot)[:, :, None], g_win, jnp.zeros((), g_win.dtype))
    q_slots = q_slots.reshape(slot_count, STRETCH, head_count, head_depth)
    g_slots = g_slots.reshape(slot_count, STRETCH, head_count, head_depth)

    stored = neighbour_kv[0]
    key_rows = stored[:, :, 0].reshape(slot_count, NB_LEN, head_count, head_depth)
    value_rows = stored[:, :, 1].reshape(slot_count, NB_LEN, head_count, head_depth)
    scores = jnp.einsum("sihd,sjhd->sihj", q_slots, key_rows, preferred_element_type=jnp.float32)
    scores = scores * scale_factor + bias_rows[None]
    peak_val = jnp.max(scores, axis=-1)
    weights = jnp.exp(scores - peak_val[..., None])
    row_total = jnp.sum(weights, axis=-1)
    partial_value = jnp.einsum(
        "sihj,sjhd->sihd",
        weights.astype(jnp.bfloat16),
        value_rows,
        preferred_element_type=jnp.float32,
    )

    owner_of = jnp.where(is_used, my_targets // per_owner, -1)
    owner_match = owner_of[None, :] == jnp.arange(shard_count)[:, None]
    send_slot = jnp.argmax(owner_match, axis=1)
    send_has = jnp.any(owner_match, axis=1)
    part_send = take_rows(
        partial_value.astype(jnp.bfloat16).reshape(slot_count, STRETCH, width_dev), send_slot, send_has
    )
    g_dot = jnp.einsum(
        "sihd,sihd->sih", g_slots.astype(jnp.float32), partial_value, precision=lax.Precision.HIGHEST
    )
    mine = jnp.stack([peak_val, row_total, g_dot], axis=1)
    shared = jnp.concatenate(
        [mine.reshape(slot_count, -1), jnp.where(is_used, entry + 1, 0).astype(jnp.float32)[:, None]],
        axis=1,
    )
    shared_wide = jnp.pad(shared, ((0, 0), (0, 1024 - shared.shape[1])))
    shared_all = lax.all_gather(shared_wide, "seq", tiled=True)[:, : shared.shape[1]]
    partner = entry + 1 - 2 * (entry % 2)
    partner_at = jnp.argmax(shared_all[None, :, -1] == (partner + 1).astype(jnp.float32)[:, None], axis=1)
    theirs = jnp.take(shared_all[:, :-1], partner_at, axis=0).reshape(mine.shape)
    both_peak = jnp.maximum(mine[:, 0], theirs[:, 0])
    mine_f = jnp.exp(mine[:, 0] - both_peak)
    theirs_f = jnp.exp(theirs[:, 0] - both_peak)
    both_total = mine_f * mine[:, 1] + theirs_f * theirs[:, 1]
    lse_slots = both_peak + jnp.log(both_total)
    dd_slots = (mine_f * mine[:, 2] + theirs_f * theirs[:, 2]) / both_total
    dd_slots = jnp.where(is_used[:, None, None], dd_slots, 0.0)

    part_recv = exchange(part_send)

    own_entries = my_index * per_owner + jnp.arange(per_owner)
    own_at = jnp.argmax(shared_all[None, :, -1] == (own_entries + 1).astype(jnp.float32)[:, None], axis=1)
    held_by = own_at // slot_count
    parts_own = jnp.take(part_recv, held_by, axis=0).astype(jnp.float32)
    parts_own = parts_own.reshape(stretch_count, 2, STRETCH, head_count, head_depth)
    stats_own = jnp.take(shared_all[:, :-1], own_at, axis=0).reshape(stretch_count, 2, 3, STRETCH, head_count)
    peaks_own = stats_own[:, :, 0]
    totals_own = stats_own[:, :, 1]

    stretch_ids = my_index * stretch_count + jnp.arange(stretch_count)
    is_live = (row_ids[None, :] == 0) | ((stretch_ids[:, None] + 1) % seq_stretches != 0)
    live_rows = is_live.astype(jnp.float32)
    top_peak = jnp.max(peaks_own, axis=1)
    factor = jnp.exp(peaks_own - top_peak[:, None])
    denominator = jnp.sum(factor * totals_own, axis=1)
    combined = jnp.sum(factor[..., None] * parts_own, axis=1) / denominator[..., None]
    combined = combined * live_rows[:, :, None, None]
    att_win = combined.astype(jnp.bfloat16).reshape(tok_rows, width_dev)
    att_before = passed_along(att_win[tok_rows - STRETCH :], "seq", 1)

    prob_full = jnp.exp(scores - lse_slots[..., None])
    prob_low = prob_full.astype(jnp.bfloat16)
    grad_prob = jnp.einsum(
        "sihd,sjhd->sihj", g_slots, value_rows, preferred_element_type=jnp.float32
    )
    grad_scores = prob_full * (grad_prob - dd_slots[..., None])
    scores_low = grad_scores.astype(jnp.bfloat16)
    grad_rows = (
        jnp.einsum("sihj,sjhd->sihd", scores_low, key_rows, preferred_element_type=jnp.float32)
        * scale_factor
    )
    mix_probs = jnp.stack([scores_low, prob_low], axis=1)
    mix_rows = jnp.stack([q_slots, g_slots], axis=1)
    grad_kv = jnp.einsum("sxihj,sxihd->sjxhd", mix_probs, mix_rows, preferred_element_type=jnp.float32)
    kv_scale = jnp.array([scale_factor, 1.0], jnp.float32)[None, None, :, None, None]
    d_kv = (grad_kv * kv_scale).astype(jnp.bfloat16).reshape(slot_count, NB_LEN, 2, width_dev)
    bias_part = bias_fold(jnp.sum(grad_scores, axis=0).transpose(1, 0, 2))

    dq_rows = jnp.zeros((shard_count, stretch_count, STRETCH, width_dev), jnp.bfloat16)
    dq_owner = jnp.where(is_used, owner_of, shard_count)
    dq_rows = dq_rows.at[dq_owner, stretch_of % stretch_count].set(
        grad_rows.astype(jnp.bfloat16).reshape(slot_count, STRETCH, width_dev), mode="drop"
    )
    grad_win = lax.psum_scatter(dq_rows, "seq", scatter_dimension=0, tiled=True)
    grad_win = grad_win.reshape(tok_rows, width_dev)
    grad_before = passed_along(grad_win[tok_rows - STRETCH :], "seq", 1)
    attended = jnp.concatenate([att_before[1:], att_win[: tok_rows - STRETCH + 1]])
    d_query = jnp.concatenate([grad_before[1:], grad_win[: tok_rows - STRETCH + 1]])

    raw_sum = lax.psum(lax.psum(bias_part, "seq"), "grp")
    squares = lax.psum(jnp.sum(raw_sum * raw_sum), "mp")
    d_bias = raw_sum * jnp.minimum(1.0, 1.0 / jnp.sqrt(squares + 1e-12))
    return (attended[None], d_query[None], d_kv[None], d_bias)


def solution(mesh):
    in_specs = (
        P("grp", "seq", "mp"),
        P("grp", "seq", "mp"),
        P("grp", "seq", None, None, "mp"),
        P("grp", "seq"),
        P("mp", None),
    )
    out_specs = (
        P("grp", "seq", "mp"),
        P("grp", "seq", "mp"),
        P("grp", "seq", None, None, "mp"),
        P("mp", None),
    )
    return jax.shard_map(local, mesh=mesh, in_specs=in_specs, out_specs=out_specs, check_vma=False)
```

```python
import jax
import jax.numpy as jnp
from jax import lax
from jax.sharding import PartitionSpec as P

STRETCH = 64
NB_LEN = 128
SEQ_LEN = 2048


def passed_along(block, axis, distance):
    devices = range(lax.axis_size(axis))
    route = [(i - distance, i) for i in devices if i - distance in devices]
    return lax.ppermute(block, axis, route)


def bias_grid(lookup, row_count, col_count):
    head_num = lookup.shape[0]
    span = row_count + col_count
    padded = jnp.pad(lookup, ((0, 0), (0, 1)))
    flattened = jnp.tile(padded, (1, row_count))
    flattened = jnp.pad(flattened, ((0, 0), (0, row_count)))
    shaped = flattened.reshape(head_num, row_count, span + 1)[:, :, :col_count]
    return shaped[:, :, ::-1]


def bias_fold(grads):
    head_num, row_count, col_count = grads.shape
    turned = grads[:, :, ::-1]
    padded = jnp.pad(turned, ((0, 0), (0, 0), (0, row_count)))
    flattened = padded.reshape(head_num, row_count * (row_count + col_count))
    flattened = flattened[:, : row_count * (row_count + col_count - 1)]
    return jnp.sum(flattened.reshape(head_num, row_count, row_count + col_count - 1), axis=1)


def take_rows(table, index, valid):
    rows = jnp.take(table, index, axis=0)
    shape = (valid.shape[0],) + (1,) * (rows.ndim - 1)
    return jnp.where(valid.reshape(shape), rows, jnp.zeros((), rows.dtype))


def exchange(block):
    return lax.all_to_all(block, "seq", split_axis=0, concat_axis=0, tiled=True)


def local(queries, d_out, neighbour_kv, target, bias):
    tok_rows = queries.shape[1]
    width_dev = queries.shape[2]
    head_count = bias.shape[0]
    head_depth = width_dev // head_count
    stretch_count = tok_rows // STRETCH
    per_owner = 2 * stretch_count
    shard_count = lax.axis_size("seq")
    my_index = lax.axis_index("seq")
    group_rows = tok_rows * shard_count
    seq_stretches = min(SEQ_LEN, group_rows) // STRETCH
    scale_factor = head_depth ** (-0.5)
    bias_rows = bias_grid(bias, STRETCH, NB_LEN).transpose(1, 0, 2)
    row_ids = jnp.arange(STRETCH)

    pair = jnp.stack([queries[0], d_out[0]], axis=1)
    pair_all = lax.all_gather(pair, "seq", axis=0, tiled=True)

    my_targets = target[0]
    slot_count = my_targets.shape[0]
    is_used = my_targets >= 0
    entry = jnp.where(is_used, my_targets, 0)
    stretch_of = entry // 2
    win_rows = stretch_of[:, None] * STRETCH + (STRETCH - 1) + row_ids[None, :]
    in_group = win_rows < group_rows
    win_rows = jnp.minimum(win_rows.reshape(-1), group_rows - 1)
    win = jnp.take(pair_all, win_rows, axis=0).reshape(slot_count, STRETCH, 2, width_dev)
    q_win = win[:, :, 0]
    g_win = win[:, :, 1]
    live_slot = (row_ids[None, :] == 0) | ((stretch_of[:, None] + 1) % seq_stretches != 0)
    q_keep = is_used[:, None] & in_group
    q_slots = jnp.where(q_keep[:, :, None], q_win, jnp.zeros((), q_win.dtype))
    g_slots = jnp.where((q_keep & live_slot)[:, :, None], g_win, jnp.zeros((), g_win.dtype))
    q_slots = q_slots.reshape(slot_count, STRETCH, head_count, head_depth)
    g_slots = g_slots.reshape(slot_count, STRETCH, head_count, head_depth)

    stored = neighbour_kv[0]
    key_rows = stored[:, :, 0].reshape(slot_count, NB_LEN, head_count, head_depth)
    value_rows = stored[:, :, 1].reshape(slot_count, NB_LEN, head_count, head_depth)
    scores = jnp.einsum("sihd,sjhd->sihj", q_slots, key_rows, preferred_element_type=jnp.float32)
    scores = scores * scale_factor + bias_rows[None]
    peak_val = jnp.max(scores, axis=-1)
    weights = jnp.exp(scores - peak_val[..., None])
    row_total = jnp.sum(weights, axis=-1)
    partial_value = jnp.einsum(
        "sihj,sjhd->sihd",
        weights.astype(jnp.bfloat16),
        value_rows,
        preferred_element_type=jnp.float32,
    )

    owner_of = jnp.where(is_used, my_targets // per_owner, -1)
    owner_match = owner_of[None, :] == jnp.arange(shard_count)[:, None]
    send_slot = jnp.argmax(owner_match, axis=1)
    send_has = jnp.any(owner_match, axis=1)
    part_send = take_rows(
        partial_value.astype(jnp.bfloat16).reshape(slot_count, STRETCH, width_dev), send_slot, send_has
    )
    g_dot = jnp.einsum(
        "sihd,sihd->sih", g_slots.astype(jnp.float32), partial_value, precision=lax.Precision.HIGHEST
    )
    mine = jnp.stack([peak_val, row_total, g_dot], axis=1)
    shared = jnp.concatenate(
        [mine.reshape(slot_count, -1), jnp.where(is_used, entry + 1, 0).astype(jnp.float32)[:, None]],
        axis=1,
    )
    shared_wide = jnp.pad(shared, ((0, 0), (0, 1024 - shared.shape[1])))
    shared_all = lax.all_gather(shared_wide, "seq", tiled=True)[:, : shared.shape[1]]
    partner = entry + 1 - 2 * (entry % 2)
    partner_at = jnp.argmax(shared_all[None, :, -1] == (partner + 1).astype(jnp.float32)[:, None], axis=1)
    theirs = jnp.take(shared_all[:, :-1], partner_at, axis=0).reshape(mine.shape)
    both_peak = jnp.maximum(mine[:, 0], theirs[:, 0])
    mine_f = jnp.exp(mine[:, 0] - both_peak)
    theirs_f = jnp.exp(theirs[:, 0] - both_peak)
    both_total = mine_f * mine[:, 1] + theirs_f * theirs[:, 1]
    lse_slots = both_peak + jnp.log(both_total)
    dd_slots = (mine_f * mine[:, 2] + theirs_f * theirs[:, 2]) / both_total
    dd_slots = jnp.where(is_used[:, None, None], dd_slots, 0.0)

    part_send, shared_all = lax.optimization_barrier((part_send, shared_all))
    part_recv = exchange(part_send)

    own_entries = my_index * per_owner + jnp.arange(per_owner)
    own_at = jnp.argmax(shared_all[None, :, -1] == (own_entries + 1).astype(jnp.float32)[:, None], axis=1)
    held_by = own_at // slot_count
    parts_own = jnp.take(part_recv, held_by, axis=0).astype(jnp.float32)
    parts_own = parts_own.reshape(stretch_count, 2, STRETCH, head_count, head_depth)
    stats_own = jnp.take(shared_all[:, :-1], own_at, axis=0).reshape(stretch_count, 2, 3, STRETCH, head_count)
    peaks_own = stats_own[:, :, 0]
    totals_own = stats_own[:, :, 1]

    stretch_ids = my_index * stretch_count + jnp.arange(stretch_count)
    is_live = (row_ids[None, :] == 0) | ((stretch_ids[:, None] + 1) % seq_stretches != 0)
    live_rows = is_live.astype(jnp.float32)
    top_peak = jnp.max(peaks_own, axis=1)
    factor = jnp.exp(peaks_own - top_peak[:, None])
    denominator = jnp.sum(factor * totals_own, axis=1)
    combined = jnp.sum(factor[..., None] * parts_own, axis=1) / denominator[..., None]
    combined = combined * live_rows[:, :, None, None]
    att_win = combined.astype(jnp.bfloat16).reshape(tok_rows, width_dev)
    att_before = passed_along(att_win[tok_rows - STRETCH :], "seq", 1)

    prob_full = jnp.exp(scores - lse_slots[..., None])
    prob_low = prob_full.astype(jnp.bfloat16)
    grad_prob = jnp.einsum(
        "sihd,sjhd->sihj", g_slots, value_rows, preferred_element_type=jnp.float32
    )
    grad_scores = prob_full * (grad_prob - dd_slots[..., None])
    scores_low = grad_scores.astype(jnp.bfloat16)
    grad_rows = (
        jnp.einsum("sihj,sjhd->sihd", scores_low, key_rows, preferred_element_type=jnp.float32)
        * scale_factor
    )
    mix_probs = jnp.stack([scores_low, prob_low], axis=1)
    mix_rows = jnp.stack([q_slots, g_slots], axis=1)
    grad_kv = jnp.einsum("sxihj,sxihd->sjxhd", mix_probs, mix_rows, preferred_element_type=jnp.float32)
    kv_scale = jnp.array([scale_factor, 1.0], jnp.float32)[None, None, :, None, None]
    d_kv = (grad_kv * kv_scale).astype(jnp.bfloat16).reshape(slot_count, NB_LEN, 2, width_dev)
    bias_part = bias_fold(jnp.sum(grad_scores, axis=0).transpose(1, 0, 2))

    dq_rows = jnp.zeros((shard_count, stretch_count, STRETCH, width_dev), jnp.bfloat16)
    dq_owner = jnp.where(is_used, owner_of, shard_count)
    dq_rows = dq_rows.at[dq_owner, stretch_of % stretch_count].set(
        grad_rows.astype(jnp.bfloat16).reshape(slot_count, STRETCH, width_dev), mode="drop"
    )
    grad_win = lax.psum_scatter(dq_rows, "seq", scatter_dimension=0, tiled=True)
    grad_win = grad_win.reshape(tok_rows, width_dev)
    grad_before = passed_along(grad_win[tok_rows - STRETCH :], "seq", 1)
    attended = jnp.concatenate([att_before[1:], att_win[: tok_rows - STRETCH + 1]])
    d_query = jnp.concatenate([grad_before[1:], grad_win[: tok_rows - STRETCH + 1]])

    raw_sum = lax.psum(lax.psum(bias_part, "seq"), "grp")
    squares = lax.psum(jnp.sum(raw_sum * raw_sum), "mp")
    d_bias = raw_sum * jnp.minimum(1.0, 1.0 / jnp.sqrt(squares + 1e-12))
    return (attended[None], d_query[None], d_kv[None], d_bias)


def solution(mesh):
    in_specs = (
        P("grp", "seq", "mp"),
        P("grp", "seq", "mp"),
        P("grp", "seq", None, None, "mp"),
        P("grp", "seq"),
        P("mp", None),
    )
    out_specs = (
        P("grp", "seq", "mp"),
        P("grp", "seq", "mp"),
        P("grp", "seq", None, None, "mp"),
        P("mp", None),
    )
    return jax.shard_map(local, mesh=mesh, in_specs=in_specs, out_specs=out_specs, check_vma=False)
```
